256 devices in a mesh: grp: 4 (over y_lo, core), shard: 64 (over z, x, y_hi).
Axes of the slice: x: 4, y: 4 (y_hi: 2, y_lo: 2; y = y_hi * 2 + y_lo), z: 8, core: 2. Of those that a mesh axis runs over, the one named last changes fastest.
Arguments:
- layer_inner: float32 [4, 1600, 1600], P('grp', 'shard'), may hold values from -6 to 6
- layer_weights: float32 [1600, 1600], P('shard'), may hold values from -6 to 6
- layer_moment: float32 [1600, 1600], P('shard'), may hold values from -6 to 6
- embed_inner: float32 [4, 25600, 1600], P('grp', 'shard'), may hold values from -6 to 6
- embed_weights: float32 [25600, 1600], P(('shard', 'grp')), may hold values from -6 to 6
- embed_moment: float32 [25600, 1600], P(('shard', 'grp')), may hold values from -6 to 6
- basis: float32 [1600, 64], replicated, may hold values from -0.15625 to 0.15625
Outputs:
- layer_new: float32 [1600, 1600], P('shard')
- layer_moment_new: float32 [1600, 1600], P('shard')
- layer_copy: bfloat16 [1600, 1600], replicated
- embed_new: float32 [25600, 1600], P(('shard', 'grp'))
- embed_moment_new: float32 [25600, 1600], P(('shard', 'grp'))
The draws below stay inside these ranges and needn't reach their ends.
All inputs are finite; a program needn't handle non-finite values.
Results may differ from the reference program's by a relative error of at most 0.0015.
Values may be sent and summed in bfloat16 or wider, within the bound.
No kernel may reach another device: no remote copies, remote signals or barrier semaphores. Data moves between devices by JAX's collectives and lax.ppermute only.
A program may use at most 128 MiB of HBM per device.

```python
import jax
import jax.numpy as jnp
from jax import lax

D = 1600
RANK = 64
VOCAB = 25600
GROUPS = 4


def block_levels(stream_key, extent, split, smallest, largest):
    level, own = 1.0, jax.random.fold_in(stream_key, 6)
    for dim, shards_of in split:
        steps = jnp.exp(jax.random.uniform(jax.random.fold_in(own, dim), (shards_of,), jnp.float32, smallest / len(split), largest / len(split)))
        level = level * jnp.repeat(steps, extent[dim] // shards_of).reshape([-1 if axis == dim else 1 for axis in range(len(extent))])
    return level


def noise(stream_key, extent, width, most, cuts=(), kind=jnp.bfloat16):
    array = jax.random.normal(stream_key, extent, jnp.float32) * width
    if len(cuts) > 0:
        array = block_levels(stream_key, extent, cuts, -0.22, 0.18) * array
    return jnp.clip(array, min=-most, max=most).astype(kind)


def setup_inputs(seed: int = 0) -> dict:
    streams_of = jax.random.split(jax.random.key(seed), 8)
    return {
        "layer_inner": noise(streams_of[0], (GROUPS, D, D), 1.0, 6.0, ((0, 4), (1, 64)), jnp.float32),
        "layer_weights": noise(streams_of[1], (D, D), 1.0, 6.0, ((0, 64),), jnp.float32),
        "layer_moment": noise(streams_of[2], (D, D), 1.0, 6.0, ((0, 64),), jnp.float32),
        "embed_inner": noise(streams_of[3], (GROUPS, VOCAB, D), 1.0, 6.0, ((0, 4), (1, 64)), jnp.float32),
        "embed_weights": noise(streams_of[4], (VOCAB, D), 1.0, 6.0, ((0, 256),), jnp.float32),
        "embed_moment": noise(streams_of[5], (VOCAB, D), 1.0, 6.0, ((0, 256),), jnp.float32),
        "basis": noise(streams_of[6], (D, RANK), D ** -0.5, 0.15625, (), jnp.float32),
    }


outer_rate = 0.7
momentum_coef = 0.9


def nesterov(weights, moment, average):
    moment_new = momentum_coef * moment + average
    return weights - outer_rate * (average + momentum_coef * moment_new), moment_new


def reference(layer_inner, layer_weights, layer_moment, embed_inner, embed_weights, embed_moment, basis):
    layer_delta = jnp.mean(layer_weights[None] - layer_inner, axis=0)
    layer_new, layer_moment_new = nesterov(layer_weights, layer_moment, layer_delta)
    layer_copy = layer_new.astype(jnp.bfloat16)
    differences = embed_weights[None] - embed_inner
    projected = jnp.einsum("gvd,dr->gvr", differences, basis, precision=lax.Precision.HIGHEST)
    factors = jnp.mean(projected, axis=0)
    embed_delta = jnp.dot(factors, basis.T, precision=lax.Precision.HIGHEST)
    embed_new, embed_moment_new = nesterov(embed_weights, embed_moment, embed_delta)
    return layer_new, layer_moment_new, layer_copy, embed_new, embed_moment_new
```

```python
import jax
import jax.numpy as jnp
from jax import lax
from jax.sharding import PartitionSpec as P

outer_rate = 0.7
momentum_coef = 0.9

NZ, NX, NYH = 8, 4, 2
NG = 4


def nesterov(weights, moment, average):
    moment_new = momentum_coef * moment + average
    return (weights - outer_rate * (average + momentum_coef * moment_new), moment_new)


def both(fn):
    pairs = []
    for g in range(NG):
        for s in range(NZ * NX * NYH):
            tg, ts = fn(g, s)
            pairs.append((g * NZ * NX * NYH + s, tg * NZ * NX * NYH + ts))
    return pairs


def zxy(s):
    return s // (NX * NYH), (s // NYH) % NX, s % NYH


def sidx(z, x, y):
    return (z % NZ) * NX * NYH + (x % NX) * NYH + (y % NYH)


def butterfly_sum(v):
    v = v + lax.ppermute(v, "grp", [(i, i ^ 1) for i in range(NG)])
    return v + lax.ppermute(v, "grp", [(i, i ^ 2) for i in range(NG)])


def gather_copy(blk):
    rows, d = blk.shape
    gi = lax.axis_index("grp")
    si = lax.axis_index("shard")
    z = si // (NX * NYH)
    x = (si // NYH) % NX
    yh = si % NYH
    core = gi % 2

    other = lax.ppermute(
        blk, ("grp", "shard"), both(lambda g, s: (g ^ 2, s ^ 1))
    )
    b50 = jnp.where(yh == 0, jnp.concatenate([blk, other]), jnp.concatenate([other, blk]))

    rel = [b50]
    for k in range(1, NX):
        rel.append(
            lax.ppermute(
                b50,
                "shard",
                [(sidx(zxy(s)[0], zxy(s)[1] + k, zxy(s)[2]), s) for s in range(NZ * NX * NYH)],
            )
        )
    stacked = jnp.stack(rel)
    xi = (jnp.arange(NX) - x) % NX
    b200 = jnp.take(stacked, xi, axis=0).reshape(NX * 2 * rows, d)

    def zring(g, s):
        zz, xx, yy = zxy(s)
        return g, sidx(zz - 1, xx, yy) if g % 2 == 0 else sidx(zz + 1, xx, yy)

    zpairs = both(zring)
    cur = b200
    mine = []
    for _ in range(NZ // 2 - 1):
        cur = lax.ppermute(cur, ("grp", "shard"), zpairs)
        mine.append(cur)
    half = b200.shape[0] // 2
    send_half = jnp.where(core == 0, cur[:half], cur[half:])
    mine_half = lax.ppermute(send_half, ("grp", "shard"), zpairs)
    pack = jnp.concatenate(mine + [mine_half])
    theirs = lax.ppermute(pack, "grp", [(i, i ^ 1) for i in range(NG)])

    pieces = jnp.concatenate([b200, pack, theirs]).reshape(2 * NZ, half, d)
    nb = NZ // 2 - 1
    sign = jnp.where(core == 0, 1, -1)
    pos = [2 * z, 2 * z + 1]
    for k in range(1, nb + 1):
        zz = (z + sign * k) % NZ
        pos += [2 * zz, 2 * zz + 1]
    z4 = (z + NZ // 2) % NZ
    pos.append(2 * z4 + core)
    for k in range(1, nb + 1):
        zz = (z - sign * k) % NZ
        pos += [2 * zz, 2 * zz + 1]
    pos.append(2 * z4 + 1 - core)
    pos = jnp.stack(pos)
    src = jnp.zeros((2 * NZ,), jnp.int32).at[pos].set(jnp.arange(2 * NZ, dtype=jnp.int32))
    return jnp.take(pieces, src, axis=0).reshape(2 * NZ * half, d)


def per_device(
    layer_inner, layer_weights, layer_moment, embed_inner, embed_weights, embed_moment, basis
):
    gi = lax.axis_index("grp")
    inner_proj = jnp.dot(embed_inner[0], basis, precision=lax.Precision.HIGHEST)
    q = inner_proj.shape[0] // NG
    parts = inner_proj.reshape(NG, q, -1)
    keep1 = jnp.stack([gi, gi ^ 2])
    send1 = jnp.stack([gi ^ 1, gi ^ 3])
    a = jnp.take(parts, keep1, axis=0) + lax.ppermute(
        jnp.take(parts, send1, axis=0), "grp", [(i, i ^ 1) for i in range(NG)]
    )
    mean_proj = (a[0] + lax.ppermute(a[1], "grp", [(i, i ^ 2) for i in range(NG)])) / NG
    factors = jnp.dot(embed_weights, basis, precision=lax.Precision.HIGHEST) - mean_proj
    embed_step = jnp.dot(factors, basis.T, precision=lax.Precision.HIGHEST)
    embed_new, embed_moment_new = nesterov(embed_weights, embed_moment, embed_step)

    own_diff = layer_weights - layer_inner[0]
    average = butterfly_sum(own_diff) / NG
    layer_new, layer_moment_new = nesterov(layer_weights, layer_moment, average)
    layer_copy = gather_copy(layer_new.astype(jnp.bfloat16))
    return (layer_new, layer_moment_new, layer_copy, embed_new, embed_moment_new)


def solution(mesh):
    assert mesh.shape["shard"] == NZ * NX * NYH and mesh.shape["grp"] == NG
    in_specs = (
        P("grp", "shard", None),
        P("shard", None),
        P("shard", None),
        P("grp", "shard", None),
        P(("shard", "grp"), None),
        P(("shard", "grp"), None),
        P(),
    )
    out_specs = (
        P("shard", None),
        P("shard", None),
        P(),
        P(("shard", "grp"), None),
        P(("shard", "grp"), None),
    )
    return jax.shard_map(
        per_device, mesh=mesh, in_specs=in_specs, out_specs=out_specs, check_vma=False
    )
```

```python
import jax
import jax.numpy as jnp
from jax import lax
from jax.sharding import PartitionSpec as P

outer_rate = 0.7
momentum_coef = 0.9

NZ, NX, NYH = 8, 4, 2
NG = 4


def nesterov(weights, moment, average):
    moment_new = momentum_coef * moment + average
    return (weights - outer_rate * (average + momentum_coef * moment_new), moment_new)


def both(fn):
    pairs = []
    for g in range(NG):
        for s in range(NZ * NX * NYH):
            tg, ts = fn(g, s)
            pairs.append((g * NZ * NX * NYH + s, tg * NZ * NX * NYH + ts))
    return pairs


def zxy(s):
    return s // (NX * NYH), (s // NYH) % NX, s % NYH


def sidx(z, x, y):
    return (z % NZ) * NX * NYH + (x % NX) * NYH + (y % NYH)


def butterfly_sum(v):
    v = v + lax.ppermute(v, "grp", [(i, i ^ 1) for i in range(NG)])
    return v + lax.ppermute(v, "grp", [(i, i ^ 2) for i in range(NG)])


def gather_copy(blk):
    rows, d = blk.shape
    gi = lax.axis_index("grp")
    si = lax.axis_index("shard")
    z = si // (NX * NYH)
    x = (si // NYH) % NX
    yh = si % NYH
    core = gi % 2
    swap = [(i, i ^ 1) for i in range(NG)]

    other = lax.ppermute(blk, ("grp", "shard"), both(lambda g, s: (g ^ 2, s ^ 1)))
    b50 = jnp.zeros((NYH * rows, d), blk.dtype)
    b50 = lax.dynamic_update_slice(b50, blk, (yh * rows, 0))
    b50 = lax.dynamic_update_slice(b50, other, ((1 - yh) * rows, 0))

    zb = NX * NYH * rows
    b200 = lax.dynamic_update_slice(jnp.zeros((zb, d), blk.dtype), b50, (x * NYH * rows, 0))
    for k in range(1, NX):
        got = lax.ppermute(
            b50,
            "shard",
            [(sidx(zxy(s)[0], zxy(s)[1] + k, zxy(s)[2]), s) for s in range(NZ * NX * NYH)],
        )
        b200 = lax.dynamic_update_slice(b200, got, (((x + k) % NX) * NYH * rows, 0))

    def zring(g, s):
        zz, xx, yy = zxy(s)
        return g, sidx(zz - 1, xx, yy) if g % 2 == 0 else sidx(zz + 1, xx, yy)

    zpairs = both(zring)
    sign = 1 - 2 * core
    out = lax.dynamic_update_slice(jnp.zeros((NZ * zb, d), blk.dtype), b200, (z * zb, 0))
    cur = b200
    for k in range(1, NZ // 2):
        cur = lax.ppermute(cur, ("grp", "shard"), zpairs)
        mate = lax.ppermute(cur, "grp", swap)
        out = lax.dynamic_update_slice(out, cur, (((z + sign * k) % NZ) * zb, 0))
        out = lax.dynamic_update_slice(out, mate, (((z - sign * k) % NZ) * zb, 0))
    half = zb // 2
    send_half = lax.dynamic_slice_in_dim(cur, core * half, half, 0)
    got = lax.ppermute(send_half, ("grp", "shard"), zpairs)
    mate = lax.ppermute(got, "grp", swap)
    z4 = (z + NZ // 2) % NZ
    out = lax.dynamic_update_slice(out, got, (z4 * zb + core * half, 0))
    out = lax.dynamic_update_slice(out, mate, (z4 * zb + (1 - core) * half, 0))
    return out


def per_device(
    layer_inner, layer_weights, layer_moment, embed_inner, embed_weights, embed_moment, basis
):
    gi = lax.axis_index("grp")
    inner_proj = jnp.dot(embed_inner[0], basis, precision=lax.Precision.HIGHEST)
    q = inner_proj.shape[0] // NG
    parts = inner_proj.reshape(NG, q, -1)
    keep1 = jnp.stack([gi, gi ^ 2])
    send1 = jnp.stack([gi ^ 1, gi ^ 3])
    a = jnp.take(parts, keep1, axis=0) + lax.ppermute(
        jnp.take(parts, send1, axis=0), "grp", [(i, i ^ 1) for i in range(NG)]
    )
    mean_proj = (a[0] + lax.ppermute(a[1], "grp", [(i, i ^ 2) for i in range(NG)])) / NG
    factors = jnp.dot(embed_weights, basis, precision=lax.Precision.HIGHEST) - mean_proj
    embed_step = jnp.dot(factors, basis.T, precision=lax.Precision.HIGHEST)
    embed_new, embed_moment_new = nesterov(embed_weights, embed_moment, embed_step)

    own_diff = layer_weights - layer_inner[0]
    average = butterfly_sum(own_diff) / NG
    layer_new, layer_moment_new = nesterov(layer_weights, layer_moment, average)
    layer_copy = gather_copy(layer_new.astype(jnp.bfloat16))
    return (layer_new, layer_moment_new, layer_copy, embed_new, embed_moment_new)


def solution(mesh):
    assert mesh.shape["shard"] == NZ * NX * NYH and mesh.shape["grp"] == NG
    in_specs = (
        P("grp", "shard", None),
        P("shard", None),
        P("shard", None),
        P("grp", "shard", None),
        P(("shard", "grp"), None),
        P(("shard", "grp"), None),
        P(),
    )
    out_specs = (
        P("shard", None),
        P("shard", None),
        P(),
        P(("shard", "grp"), None),
        P(("shard", "grp"), None),
    )
    return jax.shard_map(
        per_device, mesh=mesh, in_specs=in_specs, out_specs=out_specs, check_vma=False
    )
```

```python
import jax
import jax.numpy as jnp
from jax import lax
from jax.sharding import PartitionSpec as P

outer_rate = 0.7
momentum_coef = 0.9

NZ, NX, NYH = 8, 4, 2
NG = 4


def nesterov(weights, moment, average):
    moment_new = momentum_coef * moment + average
    return (weights - outer_rate * (average + momentum_coef * moment_new), moment_new)


def both(fn):
    pairs = []
    for g in range(NG):
        for s in range(NZ * NX * NYH):
            tg, ts = fn(g, s)
            pairs.append((g * NZ * NX * NYH + s, tg * NZ * NX * NYH + ts))
    return pairs


def zxy(s):
    return s // (NX * NYH), (s // NYH) % NX, s % NYH


def sidx(z, x, y):
    return (z % NZ) * NX * NYH + (x % NX) * NYH + (y % NYH)


def butterfly_sum(v):
    v = v + lax.ppermute(v, "grp", [(i, i ^ 1) for i in range(NG)])
    return v + lax.ppermute(v, "grp", [(i, i ^ 2) for i in range(NG)])


def gather_copy(blk):
    rows, d = blk.shape
    gi = lax.axis_index("grp")
    si = lax.axis_index("shard")
    z = si // (NX * NYH)
    xy = si % (NX * NYH)
    core = gi % 2
    ns = NZ * NX * NYH
    swap = [(i, i ^ 1) for i in range(NG)]

    rel = [blk]
    for k in range(1, NX * NYH):
        def src_of(g, s, k=k):
            zz, xx, yy = zxy(s)
            dx, dy = k // NYH, k % NYH
            return (g ^ 2 if dy else g), sidx(zz, xx + dx, yy + dy)

        pairs = []
        for g in range(NG):
            for s in range(ns):
                sg, ss = src_of(g, s)
                pairs.append((sg * ns + ss, g * ns + s))
        rel.append(lax.ppermute(blk, ("grp", "shard"), pairs))
    stacked = jnp.stack(rel)
    x = xy // NYH
    yh = xy % NYH
    k_of = []
    for a in range(NX * NYH):
        ax, ay = a // NYH, a % NYH
        k_of.append(((ax - x) % NX) * NYH + (ay - yh) % NYH)
    zb = NX * NYH * rows
    b200 = jnp.take(stacked, jnp.stack(k_of), axis=0).reshape(zb, d)

    def zring(g, s):
        zz, xx, yy = zxy(s)
        return g, sidx(zz - 1, xx, yy) if g % 2 == 0 else sidx(zz + 1, xx, yy)

    zpairs = both(zring)
    cut = (d // 2) // 128 * 128
    sign = 1 - 2 * core
    out = lax.dynamic_update_slice(jnp.zeros((NZ * zb, d), blk.dtype), b200, (z * zb, 0))
    cur = [b200[:, :cut], b200[:, cut:]]
    for k in range(1, NZ // 2):
        cur = [lax.ppermute(c, ("grp", "shard"), zpairs) for c in cur]
        mate = [lax.ppermute(c, "grp", swap) for c in cur]
        mine_at = ((z + sign * k) % NZ) * zb
        mate_at = ((z - sign * k) % NZ) * zb
        for c, m, col in zip(cur, mate, (0, cut)):
            out = lax.dynamic_update_slice(out, c, (mine_at, col))
            out = lax.dynamic_update_slice(out, m, (mate_at, col))
    z4 = ((z + NZ // 2) % NZ) * zb
    first = [p for p in zpairs if (p[1] // ns) % 2 == 0]
    second = [p for p in zpairs if (p[1] // ns) % 2 == 1]
    got_a = lax.ppermute(cur[0], ("grp", "shard"), first)
    got_b = lax.ppermute(cur[1], ("grp", "shard"), second)
    sw_a = lax.ppermute(got_a, "grp", [(i, i ^ 1) for i in range(NG) if i % 2 == 0])
    sw_b = lax.ppermute(got_b, "grp", [(i, i ^ 1) for i in range(NG) if i % 2 == 1])
    got_a = jnp.where(core == 0, got_a, sw_a)
    got_b = jnp.where(core == 0, sw_b, got_b)
    out = lax.dynamic_update_slice(out, got_a, (z4, 0))
    out = lax.dynamic_update_slice(out, got_b, (z4, cut))
    return out


def per_device(
    layer_inner, layer_weights, layer_moment, embed_inner, embed_weights, embed_moment, basis
):
    gi = lax.axis_index("grp")
    inner_proj = jnp.dot(embed_inner[0], basis, precision=lax.Precision.HIGHEST)
    q = inner_proj.shape[0] // NG
    parts = inner_proj.reshape(NG, q, -1)
    keep1 = jnp.stack([gi, gi ^ 2])
    send1 = jnp.stack([gi ^ 1, gi ^ 3])
    a = jnp.take(parts, keep1, axis=0) + lax.ppermute(
        jnp.take(parts, send1, axis=0), "grp", [(i, i ^ 1) for i in range(NG)]
    )
    mean_proj = (a[0] + lax.ppermute(a[1], "grp", [(i, i ^ 2) for i in range(NG)])) / NG
    factors = jnp.dot(embed_weights, basis, precision=lax.Precision.HIGHEST) - mean_proj
    embed_step = jnp.dot(factors, basis.T, precision=lax.Precision.HIGHEST)
    embed_new, embed_moment_new = nesterov(embed_weights, embed_moment, embed_step)

    own_diff = layer_weights - layer_inner[0]
    average = butterfly_sum(own_diff) / NG
    layer_new, layer_moment_new = nesterov(layer_weights, layer_moment, average)
    layer_copy = gather_copy(layer_new.astype(jnp.bfloat16))
    return (layer_new, layer_moment_new, layer_copy, embed_new, embed_moment_new)


def solution(mesh):
    assert mesh.shape["shard"] == NZ * NX * NYH and mesh.shape["grp"] == NG
    in_specs = (
        P("grp", "shard", None),
        P("shard", None),
        P("shard", None),
        P("grp", "shard", None),
        P(("shard", "grp"), None),
        P(("shard", "grp"), None),
        P(),
    )
    out_specs = (
        P("shard", None),
        P("shard", None),
        P(),
        P(("shard", "grp"), None),
        P(("shard", "grp"), None),
    )
    return jax.shard_map(
        per_device, mesh=mesh, in_specs=in_specs, out_specs=out_specs, check_vma=False
    )
```

```python
import jax
import jax.numpy as jnp
from jax import lax
from jax.sharding import PartitionSpec as P

outer_rate = 0.7
momentum_coef = 0.9

NZ, NX, NYH = 8, 4, 2
NG = 4


def nesterov(weights, moment, average):
    moment_new = momentum_coef * moment + average
    return (weights - outer_rate * (average + momentum_coef * moment_new), moment_new)


def both(fn):
    pairs = []
    for g in range(NG):
        for s in range(NZ * NX * NYH):
            tg, ts = fn(g, s)
            pairs.append((g * NZ * NX * NYH + s, tg * NZ * NX * NYH + ts))
    return pairs


def zxy(s):
    return s // (NX * NYH), (s // NYH) % NX, s % NYH


def sidx(z, x, y):
    return (z % NZ) * NX * NYH + (x % NX) * NYH + (y % NYH)


def butterfly_sum(v):
    v = v + lax.ppermute(v, "grp", [(i, i ^ 1) for i in range(NG)])
    return v + lax.ppermute(v, "grp", [(i, i ^ 2) for i in range(NG)])


def gather_copy(blk):
    rows, d = blk.shape
    gi = lax.axis_index("grp")
    si = lax.axis_index("shard")
    z = si // (NX * NYH)
    x = (si // NYH) % NX
    yh = si % NYH
    core = gi % 2
    swap = [(i, i ^ 1) for i in range(NG)]

    other = lax.ppermute(blk, ("grp", "shard"), both(lambda g, s: (g ^ 2, s ^ 1)))
    b50 = jnp.where(yh == 0, jnp.concatenate([blk, other]), jnp.concatenate([other, blk]))

    zb = NX * NYH * rows
    rel = [b50]
    for k in range(1, NX):
        rel.append(
            lax.ppermute(
                b50,
                "shard",
                [(sidx(zxy(s)[0], zxy(s)[1] + k, zxy(s)[2]), s) for s in range(NZ * NX * NYH)],
            )
        )
    xi = (jnp.arange(NX) - x) % NX
    b200 = jnp.take(jnp.stack(rel), xi, axis=0).reshape(zb, d)

    def zring(g, s):
        zz, xx, yy = zxy(s)
        return g, sidx(zz - 1, xx, yy) if g % 2 == 0 else sidx(zz + 1, xx, yy)

    zpairs = both(zring)
    sign = 1 - 2 * core
    out = lax.dynamic_update_slice(jnp.zeros((NZ * zb, d), blk.dtype), b200, (z * zb, 0))
    cur = b200
    for k in range(1, NZ // 2):
        cur = lax.ppermute(cur, ("grp", "shard"), zpairs)
        mate = lax.ppermute(cur, "grp", swap)
        out = lax.dynamic_update_slice(out, cur, (((z + sign * k) % NZ) * zb, 0))
        out = lax.dynamic_update_slice(out, mate, (((z - sign * k) % NZ) * zb, 0))
    cut = (d // 2) // 128 * 128
    width = d - cut
    send_half = lax.dynamic_slice_in_dim(cur, core * cut, width, 1)
    got = lax.ppermute(send_half, ("grp", "shard"), zpairs)
    mate = lax.ppermute(got, "grp", swap)
    z4 = ((z + NZ // 2) % NZ) * zb
    out = lax.dynamic_update_slice(out, got, (z4, core * cut))
    out = lax.dynamic_update_slice(out, mate, (z4, (1 - core) * cut))
    return out


def per_device(
    layer_inner, layer_weights, layer_moment, embed_inner, embed_weights, embed_moment, basis
):
    gi = lax.axis_index("grp")
    inner_proj = jnp.dot(embed_inner[0], basis, precision=lax.Precision.HIGHEST)
    q = inner_proj.shape[0] // NG
    parts = inner_proj.reshape(NG, q, -1)
    keep1 = jnp.stack([gi, gi ^ 2])
    send1 = jnp.stack([gi ^ 1, gi ^ 3])
    a = jnp.take(parts, keep1, axis=0) + lax.ppermute(
        jnp.take(parts, send1, axis=0), "grp", [(i, i ^ 1) for i in range(NG)]
    )
    mean_proj = (a[0] + lax.ppermute(a[1], "grp", [(i, i ^ 2) for i in range(NG)])) / NG
    factors = jnp.dot(embed_weights, basis, precision=lax.Precision.HIGHEST) - mean_proj
    embed_step = jnp.dot(factors, basis.T, precision=lax.Precision.HIGHEST)
    embed_new, embed_moment_new = nesterov(embed_weights, embed_moment, embed_step)

    own_diff = layer_weights - layer_inner[0]
    average = butterfly_sum(own_diff) / NG
    layer_new, layer_moment_new = nesterov(layer_weights, layer_moment, average)
    layer_copy = gather_copy(layer_new.astype(jnp.bfloat16))
    return (layer_new, layer_moment_new, layer_copy, embed_new, embed_moment_new)


def solution(mesh):
    assert mesh.shape["shard"] == NZ * NX * NYH and mesh.shape["grp"] == NG
    in_specs = (
        P("grp", "shard", None),
        P("shard", None),
        P("shard", None),
        P("grp", "shard", None),
        P(("shard", "grp"), None),
        P(("shard", "grp"), None),
        P(),
    )
    out_specs = (
        P("shard", None),
        P("shard", None),
        P(),
        P(("shard", "grp"), None),
        P(("shard", "grp"), None),
    )
    return jax.shard_map(
        per_device, mesh=mesh, in_specs=in_specs, out_specs=out_specs, check_vma=False
    )
```

```python
import jax
import jax.numpy as jnp
from jax import lax
from jax.sharding import PartitionSpec as P

outer_rate = 0.7
momentum_coef = 0.9

NZ, NX, NYH = 8, 4, 2
NG = 4


def nesterov(weights, moment, average):
    moment_new = momentum_coef * moment + average
    return (weights - outer_rate * (average + momentum_coef * moment_new), moment_new)


def both(fn):
    pairs = []
    for g in range(NG):
        for s in range(NZ * NX * NYH):
            tg, ts = fn(g, s)
            pairs.append((g * NZ * NX * NYH + s, tg * NZ * NX * NYH + ts))
    return pairs


def zxy(s):
    return s // (NX * NYH), (s // NYH) % NX, s % NYH


def sidx(z, x, y):
    return (z % NZ) * NX * NYH + (x % NX) * NYH + (y % NYH)


def butterfly_sum(v):
    v = v + lax.ppermute(v, "grp", [(i, i ^ 1) for i in range(NG)])
    return v + lax.ppermute(v, "grp", [(i, i ^ 2) for i in range(NG)])


def gather_copy(blk):
    rows, d = blk.shape
    gi = lax.axis_index("grp")
    si = lax.axis_index("shard")
    z = si // (NX * NYH)
    x = (si // NYH) % NX
    yh = si % NYH
    core = gi % 2
    swap = [(i, i ^ 1) for i in range(NG)]
    ns = NZ * NX * NYH

    other = lax.ppermute(blk, ("grp", "shard"), both(lambda g, s: (g ^ 2, s ^ 1)))
    b50 = jnp.zeros((NYH * rows, d), blk.dtype)
    b50 = lax.dynamic_update_slice(b50, blk, (yh * rows, 0))
    b50 = lax.dynamic_update_slice(b50, other, ((1 - yh) * rows, 0))

    zb = NX * NYH * rows
    b200 = lax.dynamic_update_slice(jnp.zeros((zb, d), blk.dtype), b50, (x * NYH * rows, 0))
    for k in range(1, NX):
        got = lax.ppermute(
            b50,
            "shard",
            [(sidx(zxy(s)[0], zxy(s)[1] + k, zxy(s)[2]), s) for s in range(NZ * NX * NYH)],
        )
        b200 = lax.dynamic_update_slice(b200, got, (((x + k) % NX) * NYH * rows, 0))

    def zring(g, s):
        zz, xx, yy = zxy(s)
        return g, sidx(zz - 1, xx, yy) if g % 2 == 0 else sidx(zz + 1, xx, yy)

    zpairs = both(zring)
    cut = (d // 2) // 128 * 128
    sign = 1 - 2 * core
    out = lax.dynamic_update_slice(jnp.zeros((NZ * zb, d), blk.dtype), b200, (z * zb, 0))
    cur = [b200[:, :cut], b200[:, cut:]]
    for k in range(1, NZ // 2):
        cur = [lax.ppermute(c, ("grp", "shard"), zpairs) for c in cur]
        mate = [lax.ppermute(c, "grp", swap) for c in cur]
        mine_at = ((z + sign * k) % NZ) * zb
        mate_at = ((z - sign * k) % NZ) * zb
        for c, m, col in zip(cur, mate, (0, cut)):
            out = lax.dynamic_update_slice(out, c, (mine_at, col))
            out = lax.dynamic_update_slice(out, m, (mate_at, col))
    z4 = ((z + NZ // 2) % NZ) * zb
    first = [p for p in zpairs if (p[1] // ns) % 2 == 0]
    second = [p for p in zpairs if (p[1] // ns) % 2 == 1]
    got_a = lax.ppermute(cur[0], ("grp", "shard"), first)
    got_b = lax.ppermute(cur[1], ("grp", "shard"), second)
    sw_a = lax.ppermute(got_a, "grp", [(i, i ^ 1) for i in range(NG) if i % 2 == 0])
    sw_b = lax.ppermute(got_b, "grp", [(i, i ^ 1) for i in range(NG) if i % 2 == 1])
    got_a = jnp.where(core == 0, got_a, sw_a)
    got_b = jnp.where(core == 0, sw_b, got_b)
    out = lax.dynamic_update_slice(out, got_a, (z4, 0))
    out = lax.dynamic_update_slice(out, got_b, (z4, cut))
    return out


def per_device(
    layer_inner, layer_weights, layer_moment, embed_inner, embed_weights, embed_moment, basis
):
    gi = lax.axis_index("grp")
    inner_proj = jnp.dot(embed_inner[0], basis, precision=lax.Precision.HIGHEST)
    q = inner_proj.shape[0] // NG
    parts = inner_proj.reshape(NG, q, -1)
    keep1 = jnp.stack([gi, gi ^ 2])
    send1 = jnp.stack([gi ^ 1, gi ^ 3])
    a = jnp.take(parts, keep1, axis=0) + lax.ppermute(
        jnp.take(parts, send1, axis=0), "grp", [(i, i ^ 1) for i in range(NG)]
    )
    mean_proj = (a[0] + lax.ppermute(a[1], "grp", [(i, i ^ 2) for i in range(NG)])) / NG
    factors = jnp.dot(embed_weights, basis, precision=lax.Precision.HIGHEST) - mean_proj
    embed_step = jnp.dot(factors, basis.T, precision=lax.Precision.HIGHEST)
    embed_new, embed_moment_new = nesterov(embed_weights, embed_moment, embed_step)

    own_diff = layer_weights - layer_inner[0]
    average = butterfly_sum(own_diff) / NG
    layer_new, layer_moment_new = nesterov(layer_weights, layer_moment, average)
    layer_copy = gather_copy(layer_new.astype(jnp.bfloat16))
    return (layer_new, layer_moment_new, layer_copy, embed_new, embed_moment_new)


def solution(mesh):
    assert mesh.shape["shard"] == NZ * NX * NYH and mesh.shape["grp"] == NG
    in_specs = (
        P("grp", "shard", None),
        P("shard", None),
        P("shard", None),
        P("grp", "shard", None),
        P(("shard", "grp"), None),
        P(("shard", "grp"), None),
        P(),
    )
    out_specs = (
        P("shard", None),
        P("shard", None),
        P(),
        P(("shard", "grp"), None),
        P(("shard", "grp"), None),
    )
    return jax.shard_map(
        per_device, mesh=mesh, in_specs=in_specs, out_specs=out_specs, check_vma=False
    )
```

```python
import jax
import jax.numpy as jnp
from jax import lax
from jax.sharding import PartitionSpec as P


outer_rate = 0.7
momentum_coef = 0.9

NZ, NX, NYH = 8, 4, 2
NG = 4


def nesterov(weights, moment, average):
    moment_new = momentum_coef * moment + average
    return (weights - outer_rate * (average + momentum_coef * moment_new), moment_new)


def both(fn):
    pairs = []
    for g in range(NG):
        for s in range(NZ * NX * NYH):
            tg, ts = fn(g, s)
            pairs.append((g * NZ * NX * NYH + s, tg * NZ * NX * NYH + ts))
    return pairs


def zxy(s):
    return s // (NX * NYH), (s // NYH) % NX, s % NYH


def sidx(z, x, y):
    return (z % NZ) * NX * NYH + (x % NX) * NYH + (y % NYH)


def butterfly_sum(v):
    v = v + lax.ppermute(v, "grp", [(i, i ^ 1) for i in range(NG)])
    far = lax.ppermute(v, "grp", [(i, i ^ 2) for i in range(NG)])
    return v + far


def gather_copy(blk):
    rows, d = blk.shape
    gi = lax.axis_index("grp")
    si = lax.axis_index("shard")
    z = si // (NX * NYH)
    x = (si // NYH) % NX
    yh = si % NYH
    core = gi % 2
    swap = [(i, i ^ 1) for i in range(NG)]
    ns = NZ * NX * NYH

    other = lax.ppermute(blk, ("grp", "shard"), both(lambda g, s: (g ^ 2, s ^ 1)))
    b50 = jnp.zeros((NYH * rows, d), blk.dtype)
    b50 = lax.dynamic_update_slice(b50, blk, (yh * rows, 0))
    b50 = lax.dynamic_update_slice(b50, other, ((1 - yh) * rows, 0))

    zb = NX * NYH * rows
    b200 = lax.dynamic_update_slice(jnp.zeros((zb, d), blk.dtype), b50, (x * NYH * rows, 0))
    for k in range(1, NX):
        got = lax.ppermute(
            b50,
            "shard",
            [(sidx(zxy(s)[0], zxy(s)[1] + k, zxy(s)[2]), s) for s in range(NZ * NX * NYH)],
        )
        b200 = lax.dynamic_update_slice(b200, got, (((x + k) % NX) * NYH * rows, 0))

    def zring(g, s):
        zz, xx, yy = zxy(s)
        return g, sidx(zz - 1, xx, yy) if g % 2 == 0 else sidx(zz + 1, xx, yy)

    zpairs = both(zring)
    cut = (d // 2) // 128 * 128
    sign = 1 - 2 * core
    out = lax.dynamic_update_slice(jnp.zeros((NZ * zb, d), blk.dtype), b200, (z * zb, 0))
    cur = [b200[:, :cut], b200[:, cut:]]
    for k in range(1, NZ // 2):
        cur = [lax.ppermute(c, ("grp", "shard"), zpairs) for c in cur]
        mate = [lax.ppermute(c, "grp", swap) for c in cur]
        mine_at = ((z + sign * k) % NZ) * zb
        mate_at = ((z - sign * k) % NZ) * zb
        for c, m, col in zip(cur, mate, (0, cut)):
            out = lax.dynamic_update_slice(out, c, (mine_at, col))
            out = lax.dynamic_update_slice(out, m, (mate_at, col))
    z4 = ((z + NZ // 2) % NZ) * zb
    first = [p for p in zpairs if (p[1] // ns) % 2 == 0]
    second = [p for p in zpairs if (p[1] // ns) % 2 == 1]
    got_a = lax.ppermute(cur[0], ("grp", "shard"), first)
    got_b = lax.ppermute(cur[1], ("grp", "shard"), second)
    sw_a = lax.ppermute(got_a, "grp", [(i, i ^ 1) for i in range(NG) if i % 2 == 0])
    sw_b = lax.ppermute(got_b, "grp", [(i, i ^ 1) for i in range(NG) if i % 2 == 1])
    got_a = jnp.where(core == 0, got_a, sw_a)
    got_b = jnp.where(core == 0, sw_b, got_b)
    out = lax.dynamic_update_slice(out, got_a, (z4, 0))
    out = lax.dynamic_update_slice(out, got_b, (z4, cut))
    return out


def body(layer_inner, layer_weights, layer_moment, embed_inner, embed_weights, embed_moment, basis):
    gi = lax.axis_index("grp")
    inner_proj = jnp.dot(embed_inner[0], basis, precision=lax.Precision.HIGHEST)
    own_proj = jnp.dot(embed_weights, basis, precision=lax.Precision.HIGHEST)
    q = inner_proj.shape[0] // NG
    parts = inner_proj.reshape(NG, q, -1)
    keep1 = jnp.stack([gi, gi ^ 2])
    send1 = jnp.stack([gi ^ 1, gi ^ 3])
    a = jnp.take(parts, keep1, axis=0) + lax.ppermute(
        jnp.take(parts, send1, axis=0), "grp", [(i, i ^ 1) for i in range(NG)]
    )
    mean_proj = (a[0] + lax.ppermute(a[1], "grp", [(i, i ^ 2) for i in range(NG)])) / NG
    factors = own_proj - mean_proj
    embed_step = jnp.dot(factors, basis.T, precision=lax.Precision.HIGHEST)
    embed_new, embed_moment_new = nesterov(embed_weights, embed_moment, embed_step)

    own_diff = layer_weights - layer_inner[0]
    average = butterfly_sum(own_diff) / NG
    layer_new, layer_moment_new = nesterov(layer_weights, layer_moment, average)
    layer_copy = gather_copy(layer_new.astype(jnp.bfloat16))
    return (layer_new, layer_moment_new, layer_copy, embed_new, embed_moment_new)


def solution(mesh):
    assert mesh.shape["shard"] == NZ * NX * NYH and mesh.shape["grp"] == NG
    in_specs = (
        P("grp", "shard", None),
        P("shard", None),
        P("shard", None),
        P("grp", "shard", None),
        P(("shard", "grp"), None),
        P(("shard", "grp"), None),
        P(),
    )
    out_specs = (
        P("shard", None),
        P("shard", None),
        P(),
        P(("shard", "grp"), None),
        P(("shard", "grp"), None),
    )
    return jax.shard_map(body, mesh=mesh, in_specs=in_specs, out_specs=out_specs, check_vma=False)
```

```python
import jax
import jax.numpy as jnp
from jax import lax
from jax.sharding import PartitionSpec as P


outer_rate = 0.7
momentum_coef = 0.9

NZ, NX, NYH = 8, 4, 2
NG = 4
NST = 4


def nesterov(weights, moment, average):
    moment_new = momentum_coef * moment + average
    return (weights - outer_rate * (average + momentum_coef * moment_new), moment_new)


def both(fn):
    pairs = []
    for g in range(NG):
        for s in range(NZ * NX * NYH):
            tg, ts = fn(g, s)
            pairs.append((g * NZ * NX * NYH + s, tg * NZ * NX * NYH + ts))
    return pairs


def zxy(s):
    return s // (NX * NYH), (s // NYH) % NX, s % NYH


def sidx(z, x, y):
    return (z % NZ) * NX * NYH + (x % NX) * NYH + (y % NYH)


def butterfly_sum(v):
    v = v + lax.ppermute(v, "grp", [(i, i ^ 1) for i in range(NG)])
    far = lax.ppermute(v, "grp", [(i, i ^ 2) for i in range(NG)])
    return v + far


def gather_copy(blk):
    rows, d = blk.shape
    gi = lax.axis_index("grp")
    si = lax.axis_index("shard")
    z = si // (NX * NYH)
    x = (si // NYH) % NX
    yh = si % NYH
    core = gi % 2
    swap = [(i, i ^ 1) for i in range(NG)]
    ns = NZ * NX * NYH

    other = lax.ppermute(blk, ("grp", "shard"), both(lambda g, s: (g ^ 2, s ^ 1)))
    b50 = jnp.where(yh == 0, jnp.concatenate([blk, other]), jnp.concatenate([other, blk]))

    zb = NX * NYH * rows
    rel = [b50]
    for k in range(1, NX):
        rel.append(
            lax.ppermute(
                b50,
                "shard",
                [(sidx(zxy(s)[0], zxy(s)[1] + k, zxy(s)[2]), s) for s in range(NZ * NX * NYH)],
            )
        )
    xi = (jnp.arange(NX) - x) % NX
    b200 = jnp.take(jnp.stack(rel), xi, axis=0).reshape(zb, d)

    def zring(g, s):
        zz, xx, yy = zxy(s)
        return g, sidx(zz - 1, xx, yy) if g % 2 == 0 else sidx(zz + 1, xx, yy)

    zpairs = both(zring)
    step_cols = (d // NST) // 128 * 128
    bounds = [i * step_cols for i in range(NST)] + [d]
    spans = list(zip(bounds[:-1], bounds[1:]))
    sign = 1 - 2 * core
    out = lax.dynamic_update_slice(jnp.zeros((NZ * zb, d), blk.dtype), b200, (z * zb, 0))
    cur = [b200[:, lo:hi] for lo, hi in spans]
    for k in range(1, NZ // 2):
        cur = [lax.ppermute(c, ("grp", "shard"), zpairs) for c in cur]
        mate = [lax.ppermute(c, "grp", swap) for c in cur]
        mine_at = ((z + sign * k) % NZ) * zb
        mate_at = ((z - sign * k) % NZ) * zb
        for c, m, (lo, _) in zip(cur, mate, spans):
            out = lax.dynamic_update_slice(out, c, (mine_at, lo))
            out = lax.dynamic_update_slice(out, m, (mate_at, lo))
    z4 = ((z + NZ // 2) % NZ) * zb
    first = [p for p in zpairs if (p[1] // ns) % 2 == 0]
    second = [p for p in zpairs if (p[1] // ns) % 2 == 1]
    half = NST // 2
    gots = [
        lax.ppermute(c, ("grp", "shard"), first if i < half else second)
        for i, c in enumerate(cur)
    ]
    for i, (got, (lo, _)) in enumerate(zip(gots, spans)):
        side = 0 if i < half else 1
        sw = lax.ppermute(got, "grp", [(j, j ^ 1) for j in range(NG) if j % 2 == side])
        fin = jnp.where(core == side, got, sw)
        out = lax.dynamic_update_slice(out, fin, (z4, lo))
    return out


def body(layer_inner, layer_weights, layer_moment, embed_inner, embed_weights, embed_moment, basis):
    gi = lax.axis_index("grp")
    inner_proj = jnp.dot(embed_inner[0], basis, precision=lax.Precision.HIGHEST)
    own_proj = jnp.dot(embed_weights, basis, precision=lax.Precision.HIGHEST)
    q = inner_proj.shape[0] // NG
    parts = inner_proj.reshape(NG, q, -1)
    keep1 = jnp.stack([gi, gi ^ 2])
    send1 = jnp.stack([gi ^ 1, gi ^ 3])
    a = jnp.take(parts, keep1, axis=0) + lax.ppermute(
        jnp.take(parts, send1, axis=0), "grp", [(i, i ^ 1) for i in range(NG)]
    )
    mean_proj = (a[0] + lax.ppermute(a[1], "grp", [(i, i ^ 2) for i in range(NG)])) / NG
    factors = own_proj - mean_proj
    embed_step = jnp.dot(factors, basis.T, precision=lax.Precision.HIGHEST)
    embed_new, embed_moment_new = nesterov(embed_weights, embed_moment, embed_step)

    own_diff = layer_weights - layer_inner[0]
    average = butterfly_sum(own_diff) / NG
    layer_new, layer_moment_new = nesterov(layer_weights, layer_moment, average)
    layer_copy = gather_copy(layer_new.astype(jnp.bfloat16))
    return (layer_new, layer_moment_new, layer_copy, embed_new, embed_moment_new)


def solution(mesh):
    assert mesh.shape["shard"] == NZ * NX * NYH and mesh.shape["grp"] == NG
    in_specs = (
        P("grp", "shard", None),
        P("shard", None),
        P("shard", None),
        P("grp", "shard", None),
        P(("shard", "grp"), None),
        P(("shard", "grp"), None),
        P(),
    )
    out_specs = (
        P("shard", None),
        P("shard", None),
        P(),
        P(("shard", "grp"), None),
        P(("shard", "grp"), None),
    )
    return jax.shard_map(body, mesh=mesh, in_specs=in_specs, out_specs=out_specs, check_vma=False)
```

```python
import jax
import jax.numpy as jnp
from jax import lax
from jax.sharding import PartitionSpec as P


outer_rate = 0.7
momentum_coef = 0.9

NZ, NX, NYH = 8, 4, 2
NG = 4


def nesterov(weights, moment, average):
    moment_new = momentum_coef * moment + average
    return (weights - outer_rate * (average + momentum_coef * moment_new), moment_new)


def both(fn):
    pairs = []
    for g in range(NG):
        for s in range(NZ * NX * NYH):
            tg, ts = fn(g, s)
            pairs.append((g * NZ * NX * NYH + s, tg * NZ * NX * NYH + ts))
    return pairs


def zxy(s):
    return s // (NX * NYH), (s // NYH) % NX, s % NYH


def sidx(z, x, y):
    return (z % NZ) * NX * NYH + (x % NX) * NYH + (y % NYH)


def butterfly_sum(v):
    v = v + lax.ppermute(v, "grp", [(i, i ^ 1) for i in range(NG)])
    far = lax.ppermute(v, "grp", [(i, i ^ 2) for i in range(NG)])
    return v + far


def gather_copy(blk):
    rows, d = blk.shape
    gi = lax.axis_index("grp")
    si = lax.axis_index("shard")
    z = si // (NX * NYH)
    x = (si // NYH) % NX
    yh = si % NYH
    core = gi % 2
    swap = [(i, i ^ 1) for i in range(NG)]
    ns = NZ * NX * NYH

    other = lax.ppermute(blk, ("grp", "shard"), both(lambda g, s: (g ^ 2, s ^ 1)))
    b50 = jnp.where(yh == 0, jnp.concatenate([blk, other]), jnp.concatenate([other, blk]))

    zb = NX * NYH * rows
    rel = [b50]
    for k in range(1, NX):
        rel.append(
            lax.ppermute(
                b50,
                "shard",
                [(sidx(zxy(s)[0], zxy(s)[1] + k, zxy(s)[2]), s) for s in range(NZ * NX * NYH)],
            )
        )
    xi = (jnp.arange(NX) - x) % NX
    b200 = jnp.take(jnp.stack(rel), xi, axis=0).reshape(zb, d)

    def zring(g, s):
        zz, xx, yy = zxy(s)
        return g, sidx(zz - 1, xx, yy) if g % 2 == 0 else sidx(zz + 1, xx, yy)

    zpairs = both(zring)
    cut = (d // 2) // 128 * 128
    sign = 1 - 2 * core
    out = lax.dynamic_update_slice(jnp.zeros((NZ * zb, d), blk.dtype), b200, (z * zb, 0))
    cur = [b200[:, :cut], b200[:, cut:]]
    for k in range(1, NZ // 2):
        cur = [lax.ppermute(c, ("grp", "shard"), zpairs) for c in cur]
        mate = [lax.ppermute(c, "grp", swap) for c in cur]
        mine_at = ((z + sign * k) % NZ) * zb
        mate_at = ((z - sign * k) % NZ) * zb
        for c, m, col in zip(cur, mate, (0, cut)):
            out = lax.dynamic_update_slice(out, c, (mine_at, col))
            out = lax.dynamic_update_slice(out, m, (mate_at, col))
    z4 = ((z + NZ // 2) % NZ) * zb
    first = [p for p in zpairs if (p[1] // ns) % 2 == 0]
    second = [p for p in zpairs if (p[1] // ns) % 2 == 1]
    got_a = lax.ppermute(cur[0], ("grp", "shard"), first)
    got_b = lax.ppermute(cur[1], ("grp", "shard"), second)
    sw_a = lax.ppermute(got_a, "grp", [(i, i ^ 1) for i in range(NG) if i % 2 == 0])
    sw_b = lax.ppermute(got_b, "grp", [(i, i ^ 1) for i in range(NG) if i % 2 == 1])
    got_a = jnp.where(core == 0, got_a, sw_a)
    got_b = jnp.where(core == 0, sw_b, got_b)
    out = lax.dynamic_update_slice(out, got_a, (z4, 0))
    out = lax.dynamic_update_slice(out, got_b, (z4, cut))
    return out


def body(layer_inner, layer_weights, layer_moment, embed_inner, embed_weights, embed_moment, basis):
    gi = lax.axis_index("grp")
    inner_proj = jnp.dot(embed_inner[0], basis, precision=lax.Precision.HIGHEST)
    own_proj = jnp.dot(embed_weights, basis, precision=lax.Precision.HIGHEST)
    q = inner_proj.shape[0] // NG
    parts = inner_proj.reshape(NG, q, -1)
    keep1 = jnp.stack([gi, gi ^ 2])
    send1 = jnp.stack([gi ^ 1, gi ^ 3])
    a = jnp.take(parts, keep1, axis=0) + lax.ppermute(
        jnp.take(parts, send1, axis=0), "grp", [(i, i ^ 1) for i in range(NG)]
    )
    mean_proj = (a[0] + lax.ppermute(a[1], "grp", [(i, i ^ 2) for i in range(NG)])) / NG
    factors = own_proj - mean_proj
    embed_step = jnp.dot(factors, basis.T, precision=lax.Precision.HIGHEST)
    embed_new, embed_moment_new = nesterov(embed_weights, embed_moment, embed_step)

    own_diff = layer_weights - layer_inner[0]
    average = butterfly_sum(own_diff) / NG
    layer_new, layer_moment_new = nesterov(layer_weights, layer_moment, average)
    layer_copy = gather_copy(layer_new.astype(jnp.bfloat16))
    return (layer_new, layer_moment_new, layer_copy, embed_new, embed_moment_new)


def solution(mesh):
    assert mesh.shape["shard"] == NZ * NX * NYH and mesh.shape["grp"] == NG
    in_specs = (
        P("grp", "shard", None),
        P("shard", None),
        P("shard", None),
        P("grp", "shard", None),
        P(("shard", "grp"), None),
        P(("shard", "grp"), None),
        P(),
    )
    out_specs = (
        P("shard", None),
        P("shard", None),
        P(),
        P(("shard", "grp"), None),
        P(("shard", "grp"), None),
    )
    return jax.shard_map(body, mesh=mesh, in_specs=in_specs, out_specs=out_specs, check_vma=False)
```

```python
import jax
import jax.numpy as jnp
from jax import lax
from jax.sharding import PartitionSpec as P


outer_rate = 0.7
momentum_coef = 0.9

NZ, NX, NYH = 8, 4, 2
NG = 4


def nesterov(weights, moment, average):
    moment_new = momentum_coef * moment + average
    return (weights - outer_rate * (average + momentum_coef * moment_new), moment_new)


def both(fn):
    pairs = []
    for g in range(NG):
        for s in range(NZ * NX * NYH):
            tg, ts = fn(g, s)
            pairs.append((g * NZ * NX * NYH + s, tg * NZ * NX * NYH + ts))
    return pairs


def zxy(s):
    return s // (NX * NYH), (s // NYH) % NX, s % NYH


def sidx(z, x, y):
    return (z % NZ) * NX * NYH + (x % NX) * NYH + (y % NYH)


def butterfly_sum(v):
    v = v + lax.ppermute(v, "grp", [(i, i ^ 1) for i in range(NG)])
    far = lax.ppermute(v, "grp", [(i, i ^ 2) for i in range(NG)])
    return v + far


def gather_copy(blk):
    rows, d = blk.shape
    gi = lax.axis_index("grp")
    si = lax.axis_index("shard")
    z = si // (NX * NYH)
    x = (si // NYH) % NX
    yh = si % NYH
    core = gi % 2
    swap = [(i, i ^ 1) for i in range(NG)]
    ns = NZ * NX * NYH

    other = lax.ppermute(blk, ("grp", "shard"), both(lambda g, s: (g ^ 2, s ^ 1)))
    b50 = jnp.where(yh == 0, jnp.concatenate([blk, other]), jnp.concatenate([other, blk]))

    zb = NX * NYH * rows

    def xnear(g, s):
        zz, xx, yy = zxy(s)
        return g, sidx(zz, xx - 1, yy) if g % 2 == 0 else sidx(zz, xx + 1, yy)

    def xfar(g, s):
        zz, xx, yy = zxy(s)
        return g, sidx(zz, xx + 2, yy)

    cutx = (d // 2) // 128 * 128
    near = lax.ppermute(b50, ("grp", "shard"), both(xnear))
    far = lax.ppermute(
        lax.dynamic_slice_in_dim(b50, core * cutx, d - cutx, 1), ("grp", "shard"), both(xfar)
    )
    near_m = lax.ppermute(near, "grp", swap)
    far_m = lax.ppermute(far, "grp", swap)
    c0 = core == 0
    xp2 = jnp.where(
        c0,
        jnp.concatenate([far[:, :cutx], far_m], 1),
        jnp.concatenate([far_m[:, :cutx], far], 1),
    )
    rel = [b50, jnp.where(c0, near, near_m), xp2, jnp.where(c0, near_m, near)]
    xi = (jnp.arange(NX) - x) % NX
    b200 = jnp.take(jnp.stack(rel), xi, axis=0).reshape(zb, d)

    def zring(g, s):
        zz, xx, yy = zxy(s)
        return g, sidx(zz - 1, xx, yy) if g % 2 == 0 else sidx(zz + 1, xx, yy)

    zpairs = both(zring)
    cut = (d // 2) // 128 * 128
    sign = 1 - 2 * core
    out = lax.dynamic_update_slice(jnp.zeros((NZ * zb, d), blk.dtype), b200, (z * zb, 0))
    cur = [b200[:, :cut], b200[:, cut:]]
    for k in range(1, NZ // 2):
        cur = [lax.ppermute(c, ("grp", "shard"), zpairs) for c in cur]
        mate = [lax.ppermute(c, "grp", swap) for c in cur]
        mine_at = ((z + sign * k) % NZ) * zb
        mate_at = ((z - sign * k) % NZ) * zb
        for c, m, col in zip(cur, mate, (0, cut)):
            out = lax.dynamic_update_slice(out, c, (mine_at, col))
            out = lax.dynamic_update_slice(out, m, (mate_at, col))
    z4 = ((z + NZ // 2) % NZ) * zb
    first = [p for p in zpairs if (p[1] // ns) % 2 == 0]
    second = [p for p in zpairs if (p[1] // ns) % 2 == 1]
    got_a = lax.ppermute(cur[0], ("grp", "shard"), first)
    got_b = lax.ppermute(cur[1], ("grp", "shard"), second)
    sw_a = lax.ppermute(got_a, "grp", [(i, i ^ 1) for i in range(NG) if i % 2 == 0])
    sw_b = lax.ppermute(got_b, "grp", [(i, i ^ 1) for i in range(NG) if i % 2 == 1])
    got_a = jnp.where(core == 0, got_a, sw_a)
    got_b = jnp.where(core == 0, sw_b, got_b)
    out = lax.dynamic_update_slice(out, got_a, (z4, 0))
    out = lax.dynamic_update_slice(out, got_b, (z4, cut))
    return out


def body(layer_inner, layer_weights, layer_moment, embed_inner, embed_weights, embed_moment, basis):
    gi = lax.axis_index("grp")
    inner_proj = jnp.dot(embed_inner[0], basis, precision=lax.Precision.HIGHEST)
    own_proj = jnp.dot(embed_weights, basis, precision=lax.Precision.HIGHEST)
    q = inner_proj.shape[0] // NG
    parts = inner_proj.reshape(NG, q, -1)
    keep1 = jnp.stack([gi, gi ^ 2])
    send1 = jnp.stack([gi ^ 1, gi ^ 3])
    a = jnp.take(parts, keep1, axis=0) + lax.ppermute(
        jnp.take(parts, send1, axis=0), "grp", [(i, i ^ 1) for i in range(NG)]
    )
    mean_proj = (a[0] + lax.ppermute(a[1], "grp", [(i, i ^ 2) for i in range(NG)])) / NG
    factors = own_proj - mean_proj
    embed_step = jnp.dot(factors, basis.T, precision=lax.Precision.HIGHEST)
    embed_new, embed_moment_new = nesterov(embed_weights, embed_moment, embed_step)

    own_diff = layer_weights - layer_inner[0]
    average = butterfly_sum(own_diff) / NG
    layer_new, layer_moment_new = nesterov(layer_weights, layer_moment, average)
    layer_copy = gather_copy(layer_new.astype(jnp.bfloat16))
    return (layer_new, layer_moment_new, layer_copy, embed_new, embed_moment_new)


def solution(mesh):
    assert mesh.shape["shard"] == NZ * NX * NYH and mesh.shape["grp"] == NG and NX == 4
    in_specs = (
        P("grp", "shard", None),
        P("shard", None),
        P("shard", None),
        P("grp", "shard", None),
        P(("shard", "grp"), None),
        P(("shard", "grp"), None),
        P(),
    )
    out_specs = (
        P("shard", None),
        P("shard", None),
        P(),
        P(("shard", "grp"), None),
        P(("shard", "grp"), None),
    )
    return jax.shard_map(body, mesh=mesh, in_specs=in_specs, out_specs=out_specs, check_vma=False)
```

```python
import jax
import jax.numpy as jnp
from jax import lax
from jax.sharding import PartitionSpec as P


outer_rate = 0.7
momentum_coef = 0.9

NZ, NX, NYH = 8, 4, 2
NG = 4


def nesterov(weights, moment, average):
    moment_new = momentum_coef * moment + average
    return (weights - outer_rate * (average + momentum_coef * moment_new), moment_new)


def both(fn):
    pairs = []
    for g in range(NG):
        for s in range(NZ * NX * NYH):
            tg, ts = fn(g, s)
            pairs.append((g * NZ * NX * NYH + s, tg * NZ * NX * NYH + ts))
    return pairs


def zxy(s):
    return s // (NX * NYH), (s // NYH) % NX, s % NYH


def sidx(z, x, y):
    return (z % NZ) * NX * NYH + (x % NX) * NYH + (y % NYH)


def butterfly_sum(v):
    v = v + lax.ppermute(v, "grp", [(i, i ^ 1) for i in range(NG)])
    d = v.shape[1]
    cut = (d // 2) // 128 * 128
    core = lax.axis_index("grp") % 2
    mine = lax.dynamic_slice_in_dim(v, core * cut, d - cut, 1)
    far = lax.ppermute(mine, "grp", [(i, i ^ 2) for i in range(NG)])
    part = mine + far
    other = lax.ppermute(part, "grp", [(i, i ^ 1) for i in range(NG)])
    return jnp.where(
        core == 0,
        jnp.concatenate([part[:, :cut], other], 1),
        jnp.concatenate([other[:, :cut], part], 1),
    )


def gather_copy(blk):
    rows, d = blk.shape
    gi = lax.axis_index("grp")
    si = lax.axis_index("shard")
    z = si // (NX * NYH)
    x = (si // NYH) % NX
    yh = si % NYH
    core = gi % 2
    swap = [(i, i ^ 1) for i in range(NG)]
    ns = NZ * NX * NYH

    other = lax.ppermute(blk, ("grp", "shard"), both(lambda g, s: (g ^ 2, s ^ 1)))
    b50 = jnp.where(yh == 0, jnp.concatenate([blk, other]), jnp.concatenate([other, blk]))

    zb = NX * NYH * rows

    def xnear(g, s):
        zz, xx, yy = zxy(s)
        return g, sidx(zz, xx - 1, yy) if g % 2 == 0 else sidx(zz, xx + 1, yy)

    def xfar(g, s):
        zz, xx, yy = zxy(s)
        return g, sidx(zz, xx + 2, yy)

    cutx = (d // 2) // 128 * 128
    near = lax.ppermute(b50, ("grp", "shard"), both(xnear))
    far = lax.ppermute(
        lax.dynamic_slice_in_dim(b50, core * cutx, d - cutx, 1), ("grp", "shard"), both(xfar)
    )
    near_m = lax.ppermute(near, "grp", swap)
    far_m = lax.ppermute(far, "grp", swap)
    c0 = core == 0
    xp2 = jnp.where(
        c0,
        jnp.concatenate([far[:, :cutx], far_m], 1),
        jnp.concatenate([far_m[:, :cutx], far], 1),
    )
    rel = [b50, jnp.where(c0, near, near_m), xp2, jnp.where(c0, near_m, near)]
    xi = (jnp.arange(NX) - x) % NX
    b200 = jnp.take(jnp.stack(rel), xi, axis=0).reshape(zb, d)

    def zring(g, s):
        zz, xx, yy = zxy(s)
        return g, sidx(zz - 1, xx, yy) if g % 2 == 0 else sidx(zz + 1, xx, yy)

    zpairs = both(zring)
    cut = (d // 2) // 128 * 128
    sign = 1 - 2 * core
    out = lax.dynamic_update_slice(jnp.zeros((NZ * zb, d), blk.dtype), b200, (z * zb, 0))
    cur = [b200[:, :cut], b200[:, cut:]]
    for k in range(1, NZ // 2):
        cur = [lax.ppermute(c, ("grp", "shard"), zpairs) for c in cur]
        mate = [lax.ppermute(c, "grp", swap) for c in cur]
        mine_at = ((z + sign * k) % NZ) * zb
        mate_at = ((z - sign * k) % NZ) * zb
        for c, m, col in zip(cur, mate, (0, cut)):
            out = lax.dynamic_update_slice(out, c, (mine_at, col))
            out = lax.dynamic_update_slice(out, m, (mate_at, col))
    z4 = ((z + NZ // 2) % NZ) * zb
    first = [p for p in zpairs if (p[1] // ns) % 2 == 0]
    second = [p for p in zpairs if (p[1] // ns) % 2 == 1]
    got_a = lax.ppermute(cur[0], ("grp", "shard"), first)
    got_b = lax.ppermute(cur[1], ("grp", "shard"), second)
    sw_a = lax.ppermute(got_a, "grp", [(i, i ^ 1) for i in range(NG) if i % 2 == 0])
    sw_b = lax.ppermute(got_b, "grp", [(i, i ^ 1) for i in range(NG) if i % 2 == 1])
    got_a = jnp.where(core == 0, got_a, sw_a)
    got_b = jnp.where(core == 0, sw_b, got_b)
    out = lax.dynamic_update_slice(out, got_a, (z4, 0))
    out = lax.dynamic_update_slice(out, got_b, (z4, cut))
    return out


def body(layer_inner, layer_weights, layer_moment, embed_inner, embed_weights, embed_moment, basis):
    gi = lax.axis_index("grp")
    inner_proj = jnp.dot(embed_inner[0], basis, precision=lax.Precision.HIGHEST)
    own_proj = jnp.dot(embed_weights, basis, precision=lax.Precision.HIGHEST)
    q = inner_proj.shape[0] // NG
    parts = inner_proj.reshape(NG, q, -1)
    keep1 = jnp.stack([gi, gi ^ 2])
    send1 = jnp.stack([gi ^ 1, gi ^ 3])
    a = jnp.take(parts, keep1, axis=0) + lax.ppermute(
        jnp.take(parts, send1, axis=0), "grp", [(i, i ^ 1) for i in range(NG)]
    )
    mean_proj = (a[0] + lax.ppermute(a[1], "grp", [(i, i ^ 2) for i in range(NG)])) / NG
    factors = own_proj - mean_proj
    embed_step = jnp.dot(factors, basis.T, precision=lax.Precision.HIGHEST)
    embed_new, embed_moment_new = nesterov(embed_weights, embed_moment, embed_step)

    own_diff = layer_weights - layer_inner[0]
    average = butterfly_sum(own_diff) / NG
    layer_new, layer_moment_new = nesterov(layer_weights, layer_moment, average)
    layer_copy = gather_copy(layer_new.astype(jnp.bfloat16))
    return (layer_new, layer_moment_new, layer_copy, embed_new, embed_moment_new)


def solution(mesh):
    assert mesh.shape["shard"] == NZ * NX * NYH and mesh.shape["grp"] == NG and NX == 4
    in_specs = (
        P("grp", "shard", None),
        P("shard", None),
        P("shard", None),
        P("grp", "shard", None),
        P(("shard", "grp"), None),
        P(("shard", "grp"), None),
        P(),
    )
    out_specs = (
        P("shard", None),
        P("shard", None),
        P(),
        P(("shard", "grp"), None),
        P(("shard", "grp"), None),
    )
    return jax.shard_map(body, mesh=mesh, in_specs=in_specs, out_specs=out_specs, check_vma=False)
```
